1024 devices in a mesh: row: 8 (over y, core), col: 128 (over x, z).
Axes of the slice: x: 4, y: 4, z: 32, core: 2. Of those that a mesh axis runs over, the one named last changes fastest.
Arguments:
- trailing: float32 [12288, 32768], P('row', 'col'), may hold values from -6 to 6
- leaf_v: float32 [12288, 256], P(('row', 'col')), may hold values from -0.15625 to 0.15625
- leaf_t: float32 [2048, 256], P(('row', 'col')), may hold values from -0.375 to 0.375
- tree_y: float32 [4096, 256], P(('row', 'col')), may hold values from -0.375 to 0.375
- tree_t: float32 [4096, 256], P(('row', 'col')), may hold values from -0.375 to 0.375
Outputs:
- updated: float32 [12288, 32768], P('row', 'col')
The draws below stay inside these ranges and needn't reach their ends.
All inputs are finite; a program needn't handle non-finite values.
Results may differ from the reference program's by a relative error of at most 0.00011.
Values sent between devices are 32-bit elements; how exact they have to be, the bound alone decides.
No kernel may reach another device: no remote copies, remote signals or barrier semaphores. Data moves between devices by JAX's collectives and lax.ppermute only.
A program may use at most 32 MiB of HBM per device.

```python
import jax
import jax.numpy as jnp
from jax import lax

B = 256
MB = 1536
LEVELS = 2
ORDER = 12288
NCOLS = 32768
N_ROW = 8


def levels(rng, extent, split, low, high):
    level = 1.0
    for position, parts in split:
        draws = jax.random.uniform(jax.random.fold_in(jax.random.fold_in(rng, 6), position), (parts,), jnp.float32, low / len(split), high / len(split))
        level = level * jnp.repeat(jnp.exp(draws), extent[position] // parts).reshape((-1,) + (1,) * (len(extent) - 1 - position))
    return level


def scatter_about(key, dims, spread, reach, cuts=(), kind=jnp.bfloat16):
    entries = jax.random.normal(key, dims, jnp.float32) * spread
    if len(cuts) > 0:
        entries = levels(key, dims, cuts, -0.22, 0.18) * entries
    return jnp.clip(entries, min=-reach, max=reach).astype(kind)


def setup_inputs(seed: int = 0) -> dict:
    arg_keys = jax.random.split(jax.random.key(seed), 6)
    trailing = scatter_about(arg_keys[0], (ORDER, NCOLS), 1.0, 6.0, ((0, 8), (1, 128)), jnp.float32)
    leaf_v = scatter_about(arg_keys[1], (ORDER, B), MB ** -0.5, 0.15625, ((0, 1024),), jnp.float32)
    leaf_t = scatter_about(arg_keys[2], (N_ROW * B, B), B ** -0.5, 0.375, ((0, 1024),), jnp.float32)
    tree_y = scatter_about(arg_keys[3], (N_ROW * LEVELS * B, B), B ** -0.5, 0.375, ((0, 1024),), jnp.float32)
    tree_t = scatter_about(arg_keys[4], (N_ROW * LEVELS * B, B), B ** -0.5, 0.375, ((0, 1024),), jnp.float32)
    return dict(trailing=trailing, leaf_v=leaf_v, leaf_t=leaf_t, tree_y=tree_y, tree_t=tree_t)


def unit_lower(piece, start):
    rows = start + lax.broadcasted_iota(jnp.int32, piece.shape, 0)
    cols = lax.broadcasted_iota(jnp.int32, piece.shape, 1)
    return jnp.where(rows < cols, jnp.float32(0.0), jnp.where(rows == cols, jnp.float32(1.0), piece))


def inner(left, right):
    return lax.dot_general(left, right, (((0,), (0,)), ((), ())), precision=lax.Precision.HIGHEST, preferred_element_type=jnp.float32)


def matmul(left, right):
    return jnp.dot(left, right, precision=lax.Precision.HIGHEST, preferred_element_type=jnp.float32)


def reference(trailing, leaf_v, leaf_t, tree_y, tree_t):
    tops = []
    rests = []
    for index in range(N_ROW):
        block = trailing[index * MB:(index + 1) * MB]
        vectors = unit_lower(leaf_v[index * MB:(index + 1) * MB], 0)
        factor = jnp.triu(leaf_t[index * B:(index + 1) * B])
        coeffs = inner(factor, inner(vectors, block))
        block = block - matmul(vectors, coeffs)
        tops.append(block[:B])
        rests.append(block[B:])
    for level in range(LEVELS):
        for lower in range(N_ROW):
            if (lower >> level) & 1 == 0:
                upper = lower + (1 << level)
                start_y = (lower * LEVELS + level) * B
                start_t = (upper * LEVELS + level) * B
                refl_y = tree_y[start_y:start_y + B]
                refl_t = jnp.triu(tree_t[start_t:start_t + B])
                coeffs = inner(refl_t, tops[lower] + inner(refl_y, tops[upper]))
                tops[lower] = tops[lower] - coeffs
                tops[upper] = tops[upper] - matmul(refl_y, coeffs)
    pieces = []
    for index in range(N_ROW):
        pieces.append(tops[index])
        pieces.append(rests[index])
    return jnp.concatenate(pieces, axis=0)
```

```python
import jax
import jax.numpy as jnp
from jax import lax
from jax.sharding import PartitionSpec as P


def swapped(shard, axis, stride):
    return lax.ppermute(shard, axis, [(i, i ^ 1 << stride) for i in range(lax.axis_size(axis))])


def unit_lower(piece):
    rows = lax.broadcasted_iota(jnp.int32, piece.shape, 0)
    cols = lax.broadcasted_iota(jnp.int32, piece.shape, 1)
    return jnp.where(
        rows < cols, jnp.float32(0.0), jnp.where(rows == cols, jnp.float32(1.0), piece)
    )


def inner(left, right):
    return lax.dot_general(
        left,
        right,
        (((0,), (0,)), ((), ())),
        precision=lax.Precision.HIGHEST,
        preferred_element_type=jnp.float32,
    )


def matmul(left, right):
    return jnp.dot(left, right, precision=lax.Precision.HIGHEST, preferred_element_type=jnp.float32)


def doubling_gather(shard, axis, orders):
    n = lax.axis_size(axis)
    bits = n.bit_length() - 1
    me = lax.axis_index(axis)
    width = shard.shape[1] // len(orders)
    bufs = [shard[None, :, j * width:(j + 1) * width] for j in range(len(orders))]
    for step in range(bits):
        received = [
            lax.ppermute(buf, axis, [(i, i ^ 1 << order[step]) for i in range(n)])
            for buf, order in zip(bufs, orders)
        ]
        new = []
        for buf, got, order in zip(bufs, received, orders):
            low = (me >> order[step]) & 1 == 0
            new.append(jnp.stack([jnp.where(low, buf, got), jnp.where(low, got, buf)], axis=0))
        bufs = new
    pieces = []
    for buf, order in zip(bufs, orders):
        held = list(reversed(order))
        buf = buf.reshape((2,) * bits + (shard.shape[0], width))
        buf = jnp.transpose(buf, [held.index(b) for b in range(bits - 1, -1, -1)] + [bits, bits + 1])
        pieces.append(buf.reshape(n, shard.shape[0], width))
    return jnp.concatenate(pieces, axis=2)


def combine(top_rows, refl_mine, level):
    lower_side = lax.axis_index("row") // 2**level % 2 == 0
    half = top_rows.shape[1] // 2
    first = top_rows[:, :half]
    second = top_rows[:, half:]
    kept = jnp.where(lower_side, first, second)
    outgoing = jnp.where(lower_side, second, first)
    incoming, partner_refl = swapped((outgoing, refl_mine), "row", level)
    refl_y = jnp.where(lower_side, refl_mine, partner_refl)
    refl_t = jnp.triu(jnp.where(lower_side, partner_refl, refl_mine))
    lower_top = jnp.where(lower_side, kept, incoming)
    upper_top = jnp.where(lower_side, incoming, kept)
    coeffs = inner(refl_t, lower_top + inner(refl_y, upper_top))
    new_lower = lower_top - coeffs
    new_upper = upper_top - matmul(refl_y, coeffs)
    mine = jnp.where(lower_side, new_lower, new_upper)
    theirs = jnp.where(lower_side, new_upper, new_lower)
    returned = swapped(theirs, "row", level)
    return jnp.where(
        lower_side,
        jnp.concatenate([mine, returned], axis=1),
        jnp.concatenate([returned, mine], axis=1),
    )


def local(trailing, leaf_v, leaf_t, tree_y, tree_t):
    width = leaf_v.shape[1]
    n_col = lax.axis_size("col")
    col = lax.axis_index("col")
    row = lax.axis_index("row")
    tree_depth = tree_y.shape[0] * n_col // width
    shard_level = col * tree_y.shape[0] // width
    tree_mine = jnp.where((row >> shard_level) & 1 == 0, tree_y, tree_t)
    packed = jnp.concatenate([leaf_v, leaf_t, tree_mine], axis=0)
    bits = n_col.bit_length() - 1
    high = list(range(bits - 3, -1, -1))
    orders = (high + [bits - 1, bits - 2], high[:3] + [bits - 1, bits - 2] + high[3:])
    gathered = doubling_gather(packed, "col", orders)
    nv, nt = leaf_v.shape[0], leaf_t.shape[0]
    v_rows = gathered[:, :nv].reshape(-1, width)
    t_leaf = gathered[:, nv:nv + nt].reshape(-1, width)
    tree_rows = gathered[:, nv + nt:].reshape(-1, width)
    v_rows = unit_lower(v_rows)
    coeffs = inner(jnp.triu(t_leaf), inner(v_rows, trailing))
    updated = trailing - matmul(v_rows, coeffs)
    top_rows = updated[:width]
    rest_rows = updated[width:]
    for level in range(tree_depth):
        top_rows = combine(top_rows, tree_rows[level * width:(level + 1) * width], level)
    return jnp.concatenate([top_rows, rest_rows], axis=0)


def solution(mesh):
    in_specs = (
        P("row", "col"),
        P(("row", "col"), None),
        P(("row", "col"), None),
        P(("row", "col"), None),
        P(("row", "col"), None),
    )
    out_specs = P("row", "col")
    return jax.shard_map(local, mesh=mesh, in_specs=in_specs, out_specs=out_specs, check_vma=False)
```

```python
import jax
import jax.numpy as jnp
from jax import lax
from jax.sharding import PartitionSpec as P


def swapped(shard, axis, stride):
    return lax.ppermute(shard, axis, [(i, i ^ 1 << stride) for i in range(lax.axis_size(axis))])


def unit_lower(piece):
    rows = lax.broadcasted_iota(jnp.int32, piece.shape, 0)
    cols = lax.broadcasted_iota(jnp.int32, piece.shape, 1)
    return jnp.where(
        rows < cols, jnp.float32(0.0), jnp.where(rows == cols, jnp.float32(1.0), piece)
    )


def inner(left, right):
    return lax.dot_general(
        left,
        right,
        (((0,), (0,)), ((), ())),
        precision=lax.Precision.HIGHEST,
        preferred_element_type=jnp.float32,
    )


def matmul(left, right):
    return jnp.dot(left, right, precision=lax.Precision.HIGHEST, preferred_element_type=jnp.float32)


def doubling_gather(shard, axis, orders):
    n = lax.axis_size(axis)
    bits = n.bit_length() - 1
    me = lax.axis_index(axis)
    width = shard.shape[1] // len(orders)
    bufs = [shard[:, j * width:(j + 1) * width] for j in range(len(orders))]
    held = [[] for _ in orders]
    for step in range(bits):
        received = [
            lax.ppermute(buf, axis, [(i, i ^ 1 << order[step]) for i in range(n)])
            for buf, order in zip(bufs, orders)
        ]
        for j, (got, order) in enumerate(zip(received, orders)):
            bit = order[step]
            low = (me >> bit) & 1 == 0
            pos = sum(1 for b in held[j] if b > bit)
            bufs[j] = jnp.stack([jnp.where(low, bufs[j], got), jnp.where(low, got, bufs[j])], axis=pos)
            held[j].insert(pos, bit)
    return [buf.reshape((n,) + shard.shape[:1] + (width,)) for buf in bufs]


def combine(top_rows, refl_mine, level):
    lower_side = lax.axis_index("row") // 2**level % 2 == 0
    width = top_rows.shape[0]
    incoming = swapped(jnp.concatenate([top_rows, refl_mine], axis=0), "row", level)
    partner_top, partner_refl = incoming[:width], incoming[width:]
    refl_y = jnp.where(lower_side, refl_mine, partner_refl)
    refl_t = jnp.triu(jnp.where(lower_side, partner_refl, refl_mine))
    lower_top = jnp.where(lower_side, top_rows, partner_top)
    upper_top = jnp.where(lower_side, partner_top, top_rows)
    coeffs = inner(refl_t, lower_top + inner(refl_y, upper_top))
    return jnp.where(lower_side, lower_top - coeffs, upper_top - matmul(refl_y, coeffs))


def local(trailing, leaf_v, leaf_t, tree_y, tree_t):
    width = leaf_v.shape[1]
    n_col = lax.axis_size("col")
    col = lax.axis_index("col")
    row = lax.axis_index("row")
    tree_depth = tree_y.shape[0] * n_col // width
    shard_level = col * tree_y.shape[0] // width
    tree_mine = jnp.where((row >> shard_level) & 1 == 0, tree_y, tree_t)
    packed = jnp.concatenate([leaf_v, leaf_t, tree_mine], axis=0)
    bits = n_col.bit_length() - 1
    high = list(range(bits - 3, -1, -1))
    orders = (high + [bits - 1, bits - 2], high[:3] + [bits - 1, bits - 2] + high[3:])
    pieces = doubling_gather(packed, "col", orders)
    nv, nt = leaf_v.shape[0], leaf_t.shape[0]

    def joined(lo, hi):
        return jnp.concatenate([p[:, lo:hi] for p in pieces], axis=2).reshape(-1, width)

    v_rows = unit_lower(joined(0, nv))
    t_leaf = joined(nv, nv + nt)
    tree_rows = joined(nv + nt, packed.shape[0])
    coeffs = inner(jnp.triu(t_leaf), inner(v_rows, trailing))
    updated = trailing - matmul(v_rows, coeffs)
    top_rows = updated[:width]
    for level in range(tree_depth):
        top_rows = combine(top_rows, tree_rows[level * width:(level + 1) * width], level)
    return lax.dynamic_update_slice(updated, top_rows, (0, 0))


def solution(mesh):
    in_specs = (
        P("row", "col"),
        P(("row", "col"), None),
        P(("row", "col"), None),
        P(("row", "col"), None),
        P(("row", "col"), None),
    )
    out_specs = P("row", "col")
    return jax.shard_map(local, mesh=mesh, in_specs=in_specs, out_specs=out_specs, check_vma=False)
```

```python
import jax
import jax.numpy as jnp
from jax import lax
from jax.sharding import PartitionSpec as P


def swapped(shard, axis, stride):
    return lax.ppermute(shard, axis, [(i, i ^ 1 << stride) for i in range(lax.axis_size(axis))])


def unit_lower(piece):
    rows = lax.broadcasted_iota(jnp.int32, piece.shape, 0)
    cols = lax.broadcasted_iota(jnp.int32, piece.shape, 1)
    return jnp.where(
        rows < cols, jnp.float32(0.0), jnp.where(rows == cols, jnp.float32(1.0), piece)
    )


def inner(left, right):
    return lax.dot_general(
        left,
        right,
        (((0,), (0,)), ((), ())),
        precision=lax.Precision.HIGHEST,
        preferred_element_type=jnp.float32,
    )


def matmul(left, right):
    return jnp.dot(left, right, precision=lax.Precision.HIGHEST, preferred_element_type=jnp.float32)


def doubling_gather(shard, axis, shared, orders):
    n = lax.axis_size(axis)
    me = lax.axis_index(axis)

    def step(buf, held, bit):
        got = lax.ppermute(buf, axis, [(i, i ^ 1 << bit) for i in range(n)])
        low = (me >> bit) & 1 == 0
        pos = sum(1 for b in held if b > bit)
        return jnp.stack([jnp.where(low, buf, got), jnp.where(low, got, buf)], axis=pos), held[:pos] + [bit] + held[pos:]

    buf, held = shard, []
    for bit in shared:
        buf, held = step(buf, held, bit)
    width = shard.shape[1] // len(orders)
    bufs = [buf[..., j * width:(j + 1) * width] for j in range(len(orders))]
    helds = [held] * len(orders)
    for k in range(len(orders[0])):
        for j, order in enumerate(orders):
            bufs[j], helds[j] = step(bufs[j], helds[j], order[k])
    return [b.reshape((n,) + shard.shape[:1] + (width,)) for b in bufs]


def combine(top_rows, refl_mine, partner_refl, level):
    lower_side = lax.axis_index("row") // 2**level % 2 == 0
    width = top_rows.shape[0]
    if partner_refl is None:
        incoming = swapped(jnp.concatenate([top_rows, refl_mine], axis=0), "row", level)
        partner_top, partner_refl = incoming[:width], incoming[width:]
    else:
        partner_top = swapped(top_rows, "row", level)
    refl_y = jnp.where(lower_side, refl_mine, partner_refl)
    refl_t = jnp.triu(jnp.where(lower_side, partner_refl, refl_mine))
    lower_top = jnp.where(lower_side, top_rows, partner_top)
    upper_top = jnp.where(lower_side, partner_top, top_rows)
    coeffs = inner(refl_t, lower_top + inner(refl_y, upper_top))
    return jnp.where(lower_side, lower_top - coeffs, upper_top - matmul(refl_y, coeffs))


def local(trailing, leaf_v, leaf_t, tree_y, tree_t):
    width = leaf_v.shape[1]
    n_col = lax.axis_size("col")
    col = lax.axis_index("col")
    row = lax.axis_index("row")
    tree_depth = tree_y.shape[0] * n_col // width
    shard_level = col * tree_y.shape[0] // width
    tree_mine = jnp.where((row >> shard_level) & 1 == 0, tree_y, tree_t)
    packed = jnp.concatenate([leaf_v, leaf_t, tree_mine], axis=0)
    bits = n_col.bit_length() - 1
    shared = list(range(bits - 3, 1, -1))
    orders = ([1, 0, bits - 1, bits - 2], [bits - 1, bits - 2, 1, 0])
    pieces = doubling_gather(packed, "col", shared, orders)
    nv, nt = leaf_v.shape[0], leaf_t.shape[0]

    def joined(lo, hi):
        return jnp.concatenate([p[:, lo:hi] for p in pieces], axis=2).reshape(-1, width)

    v_rows = unit_lower(joined(0, nv))
    t_leaf = joined(nv, nv + nt)
    tree_rows = joined(nv + nt, packed.shape[0])
    refl = [tree_rows[level * width:(level + 1) * width] for level in range(tree_depth)]
    partner_refl = [None] + [swapped(refl[level], "row", level) for level in range(1, tree_depth)]
    coeffs = inner(jnp.triu(t_leaf), inner(v_rows, trailing))
    updated = trailing - matmul(v_rows, coeffs)
    top_rows = updated[:width]
    for level in range(tree_depth):
        top_rows = combine(top_rows, refl[level], partner_refl[level], level)
    return lax.dynamic_update_slice(updated, top_rows, (0, 0))


def solution(mesh):
    in_specs = (
        P("row", "col"),
        P(("row", "col"), None),
        P(("row", "col"), None),
        P(("row", "col"), None),
        P(("row", "col"), None),
    )
    out_specs = P("row", "col")
    return jax.shard_map(local, mesh=mesh, in_specs=in_specs, out_specs=out_specs, check_vma=False)
```

```python
import jax
import jax.numpy as jnp
from jax import lax
from jax.sharding import PartitionSpec as P


def swapped(shard, axis, stride):
    return lax.ppermute(shard, axis, [(i, i ^ 1 << stride) for i in range(lax.axis_size(axis))])


def unit_lower(piece):
    rows = lax.broadcasted_iota(jnp.int32, piece.shape, 0)
    cols = lax.broadcasted_iota(jnp.int32, piece.shape, 1)
    return jnp.where(
        rows < cols, jnp.float32(0.0), jnp.where(rows == cols, jnp.float32(1.0), piece)
    )


def inner(left, right):
    return lax.dot_general(
        left,
        right,
        (((0,), (0,)), ((), ())),
        precision=lax.Precision.HIGHEST,
        preferred_element_type=jnp.float32,
    )


def matmul(left, right):
    return jnp.dot(left, right, precision=lax.Precision.HIGHEST, preferred_element_type=jnp.float32)


def doubling_gather(shard, axis, shared, orders):
    n = lax.axis_size(axis)
    me = lax.axis_index(axis)

    def step(buf, held, bit):
        got = lax.ppermute(buf, axis, [(i, i ^ 1 << bit) for i in range(n)])
        low = (me >> bit) & 1 == 0
        pos = sum(1 for b in held if b > bit)
        return jnp.stack([jnp.where(low, buf, got), jnp.where(low, got, buf)], axis=pos), held[:pos] + [bit] + held[pos:]

    buf, held = shard, []
    for bit in shared:
        buf, held = step(buf, held, bit)
    width = shard.shape[1] // len(orders)
    bufs = [buf[..., j * width:(j + 1) * width] for j in range(len(orders))]
    helds = [held] * len(orders)
    for k in range(len(orders[0])):
        for j, order in enumerate(orders):
            bufs[j], helds[j] = step(bufs[j], helds[j], order[k])
    return [b.reshape((n,) + shard.shape[:1] + (width,)) for b in bufs]


def combine(top_rows, refl_mine, partner_refl, level):
    lower_side = lax.axis_index("row") // 2**level % 2 == 0
    width = top_rows.shape[0]
    if partner_refl is None:
        incoming = swapped(jnp.concatenate([top_rows, refl_mine], axis=0), "row", level)
        partner_top, partner_refl = incoming[:width], incoming[width:]
    else:
        partner_top = swapped(top_rows, "row", level)
    refl_y = jnp.where(lower_side, refl_mine, partner_refl)
    refl_t = jnp.triu(jnp.where(lower_side, partner_refl, refl_mine))
    lower_top = jnp.where(lower_side, top_rows, partner_top)
    upper_top = jnp.where(lower_side, partner_top, top_rows)
    coeffs = inner(refl_t, lower_top + inner(refl_y, upper_top))
    return jnp.where(lower_side, lower_top - coeffs, upper_top - matmul(refl_y, coeffs))


def local(trailing, leaf_v, leaf_t, tree_y, tree_t):
    width = leaf_v.shape[1]
    n_col = lax.axis_size("col")
    col = lax.axis_index("col")
    row = lax.axis_index("row")
    tree_depth = tree_y.shape[0] * n_col // width
    shard_level = col * tree_y.shape[0] // width
    tree_mine = jnp.where((row >> shard_level) & 1 == 0, tree_y, tree_t)
    n_row = lax.axis_size("row")
    pairs = [
        (r * n_col + c, (r ^ 1 << (c * tree_y.shape[0] // width)) * n_col + c)
        for r in range(n_row)
        for c in range(n_col)
    ]
    tree_partner = lax.ppermute(tree_mine, ("row", "col"), pairs)
    packed = jnp.concatenate([leaf_v, leaf_t, tree_mine, tree_partner], axis=0)
    bits = n_col.bit_length() - 1
    shared = list(range(bits - 3, 1, -1))
    orders = ([1, 0, bits - 1, bits - 2], [bits - 1, bits - 2, 1, 0])
    pieces = doubling_gather(packed, "col", shared, orders)
    nv, nt = leaf_v.shape[0], leaf_t.shape[0]

    def joined(lo, hi):
        return jnp.concatenate([p[:, lo:hi] for p in pieces], axis=2).reshape(-1, width)

    v_rows = unit_lower(joined(0, nv))
    t_leaf = joined(nv, nv + nt)
    nm = tree_mine.shape[0]
    tree_rows = joined(nv + nt, nv + nt + nm)
    tree_rows_partner = joined(nv + nt + nm, packed.shape[0])
    refl = [tree_rows[level * width:(level + 1) * width] for level in range(tree_depth)]
    partner_refl = [tree_rows_partner[level * width:(level + 1) * width] for level in range(tree_depth)]
    coeffs = inner(jnp.triu(t_leaf), inner(v_rows, trailing))
    updated = trailing - matmul(v_rows, coeffs)
    top_rows = updated[:width]
    for level in range(tree_depth):
        top_rows = combine(top_rows, refl[level], partner_refl[level], level)
    return lax.dynamic_update_slice(updated, top_rows, (0, 0))


def solution(mesh):
    in_specs = (
        P("row", "col"),
        P(("row", "col"), None),
        P(("row", "col"), None),
        P(("row", "col"), None),
        P(("row", "col"), None),
    )
    out_specs = P("row", "col")
    return jax.shard_map(local, mesh=mesh, in_specs=in_specs, out_specs=out_specs, check_vma=False)
```

```python
import functools

import jax
import jax.numpy as jnp
from jax import lax
from jax.sharding import PartitionSpec as P


def swapped(shard, axis, stride):
    return lax.ppermute(shard, axis, [(i, i ^ 1 << stride) for i in range(lax.axis_size(axis))])


def unit_lower(piece):
    rows = lax.broadcasted_iota(jnp.int32, piece.shape, 0)
    cols = lax.broadcasted_iota(jnp.int32, piece.shape, 1)
    return jnp.where(
        rows < cols, jnp.float32(0.0), jnp.where(rows == cols, jnp.float32(1.0), piece)
    )


def inner(left, right):
    return lax.dot_general(
        left,
        right,
        (((0,), (0,)), ((), ())),
        precision=lax.Precision.HIGHEST,
        preferred_element_type=jnp.float32,
    )


def matmul(left, right):
    return jnp.dot(left, right, precision=lax.Precision.HIGHEST, preferred_element_type=jnp.float32)


def doubling_gather(shard, axis, label, shared, orders):
    n = lax.axis_size(axis)
    unlabel = {label(i): i for i in range(n)}
    me = label(lax.axis_index(axis))

    def step(buf, held, bit):
        got = lax.ppermute(buf, axis, [(i, unlabel[label(i) ^ 1 << bit]) for i in range(n)])
        low = (me >> bit) & 1 == 0
        pos = sum(1 for b in held if b > bit)
        return jnp.stack([jnp.where(low, buf, got), jnp.where(low, got, buf)], axis=pos), held[:pos] + [bit] + held[pos:]

    buf, held = shard, []
    for bit in shared:
        buf, held = step(buf, held, bit)
    width = shard.shape[1] // len(orders)
    bufs = [buf[..., j * width:(j + 1) * width] for j in range(len(orders))]
    helds = [held] * len(orders)
    for k in range(len(orders[0])):
        for j, order in enumerate(orders):
            bufs[j], helds[j] = step(bufs[j], helds[j], order[k])
    return [b.reshape((n,) + shard.shape[:1] + (width,)) for b in bufs]


def combine(top_rows, refl_mine, partner_refl, level):
    lower_side = lax.axis_index("row") // 2**level % 2 == 0
    width = top_rows.shape[0]
    if partner_refl is None:
        incoming = swapped(jnp.concatenate([top_rows, refl_mine], axis=0), "row", level)
        partner_top, partner_refl = incoming[:width], incoming[width:]
    else:
        partner_top = swapped(top_rows, "row", level)
    refl_y = jnp.where(lower_side, refl_mine, partner_refl)
    refl_t = jnp.triu(jnp.where(lower_side, partner_refl, refl_mine))
    lower_top = jnp.where(lower_side, top_rows, partner_top)
    upper_top = jnp.where(lower_side, partner_top, top_rows)
    coeffs = inner(refl_t, lower_top + inner(refl_y, upper_top))
    return jnp.where(lower_side, lower_top - coeffs, upper_top - matmul(refl_y, coeffs))


def local(z_len, trailing, leaf_v, leaf_t, tree_y, tree_t):
    width = leaf_v.shape[1]
    n_col = lax.axis_size("col")
    col = lax.axis_index("col")
    row = lax.axis_index("row")
    tree_depth = tree_y.shape[0] * n_col // width
    shard_level = col * tree_y.shape[0] // width
    tree_mine = jnp.where((row >> shard_level) & 1 == 0, tree_y, tree_t)
    packed = jnp.concatenate([leaf_v, leaf_t, tree_mine], axis=0)
    bits = n_col.bit_length() - 1
    z_bits = z_len.bit_length() - 1
    n_x = n_col // z_len

    def label(i):
        x = i >> z_bits
        return (x ^ x >> 1) << z_bits | i & (z_len - 1)

    shared = list(range(z_bits - 1, 0, -1))
    orders = ([0] + list(range(bits - 1, z_bits - 1, -1)), list(range(bits - 1, z_bits - 1, -1)) + [0])
    pieces = doubling_gather(packed, "col", label, shared, orders)
    nv, nt = leaf_v.shape[0], leaf_t.shape[0]
    x_order = [x ^ x >> 1 for x in range(n_x)]

    def joined(lo, hi):
        parts = []
        for p in pieces:
            groups = p[:, lo:hi].reshape(n_x, z_len, hi - lo, p.shape[2])
            parts.append(jnp.concatenate([groups[g][None] for g in x_order], axis=0))
        return jnp.concatenate(parts, axis=3).reshape(-1, width)

    v_rows = unit_lower(joined(0, nv))
    t_leaf = joined(nv, nv + nt)
    tree_rows = joined(nv + nt, packed.shape[0])
    refl = [tree_rows[level * width:(level + 1) * width] for level in range(tree_depth)]
    partner_refl = [None] + [swapped(refl[level], "row", level) for level in range(1, tree_depth)]
    coeffs = inner(jnp.triu(t_leaf), inner(v_rows, trailing))
    updated = trailing - matmul(v_rows, coeffs)
    top_rows = updated[:width]
    for level in range(tree_depth):
        top_rows = combine(top_rows, refl[level], partner_refl[level], level)
    return lax.dynamic_update_slice(updated, top_rows, (0, 0))


def solution(mesh):
    in_specs = (
        P("row", "col"),
        P(("row", "col"), None),
        P(("row", "col"), None),
        P(("row", "col"), None),
        P(("row", "col"), None),
    )
    out_specs = P("row", "col")
    z_len = len({d.coords[2] for d in mesh.devices[0].flat})
    return jax.shard_map(functools.partial(local, z_len), mesh=mesh, in_specs=in_specs, out_specs=out_specs, check_vma=False)
```

```python
import functools

import jax
import jax.numpy as jnp
from jax import lax
from jax.sharding import PartitionSpec as P


def swapped(shard, axis, stride):
    return lax.ppermute(shard, axis, [(i, i ^ 1 << stride) for i in range(lax.axis_size(axis))])


def unit_lower(piece):
    rows = lax.broadcasted_iota(jnp.int32, piece.shape, 0)
    cols = lax.broadcasted_iota(jnp.int32, piece.shape, 1)
    return jnp.where(
        rows < cols, jnp.float32(0.0), jnp.where(rows == cols, jnp.float32(1.0), piece)
    )


def inner(left, right):
    return lax.dot_general(
        left,
        right,
        (((0,), (0,)), ((), ())),
        precision=lax.Precision.HIGH,
        preferred_element_type=jnp.float32,
    )


def matmul(left, right):
    return jnp.dot(left, right, precision=lax.Precision.HIGH, preferred_element_type=jnp.float32)


def doubling_gather(shard, axis, label, shared, orders):
    n = lax.axis_size(axis)
    unlabel = {label(i): i for i in range(n)}
    me = label(lax.axis_index(axis))

    def step(buf, held, bit):
        got = lax.ppermute(buf, axis, [(i, unlabel[label(i) ^ 1 << bit]) for i in range(n)])
        low = (me >> bit) & 1 == 0
        pos = sum(1 for b in held if b > bit)
        return jnp.stack([jnp.where(low, buf, got), jnp.where(low, got, buf)], axis=pos), held[:pos] + [bit] + held[pos:]

    buf, held = shard, []
    for bit in shared:
        buf, held = step(buf, held, bit)
    width = shard.shape[1] // len(orders)
    bufs = [buf[..., j * width:(j + 1) * width] for j in range(len(orders))]
    helds = [held] * len(orders)
    for k in range(len(orders[0])):
        for j, order in enumerate(orders):
            bufs[j], helds[j] = step(bufs[j], helds[j], order[k])
    return [b.reshape((n,) + shard.shape[:1] + (width,)) for b in bufs]


def combine(top_rows, refl_mine, partner_refl, level):
    lower_side = lax.axis_index("row") // 2**level % 2 == 0
    width = top_rows.shape[0]
    if partner_refl is None:
        incoming = swapped(jnp.concatenate([top_rows, refl_mine], axis=0), "row", level)
        partner_top, partner_refl = incoming[:width], incoming[width:]
    else:
        partner_top = swapped(top_rows, "row", level)
    refl_y = jnp.where(lower_side, refl_mine, partner_refl)
    refl_t = jnp.triu(jnp.where(lower_side, partner_refl, refl_mine))
    lower_top = jnp.where(lower_side, top_rows, partner_top)
    upper_top = jnp.where(lower_side, partner_top, top_rows)
    coeffs = inner(refl_t, lower_top + inner(refl_y, upper_top))
    return jnp.where(lower_side, lower_top - coeffs, upper_top - matmul(refl_y, coeffs))


def local(z_len, trailing, leaf_v, leaf_t, tree_y, tree_t):
    width = leaf_v.shape[1]
    n_col = lax.axis_size("col")
    col = lax.axis_index("col")
    row = lax.axis_index("row")
    tree_depth = tree_y.shape[0] * n_col // width
    shard_level = col * tree_y.shape[0] // width
    tree_mine = jnp.where((row >> shard_level) & 1 == 0, tree_y, tree_t)
    packed = jnp.concatenate([leaf_v, leaf_t, tree_mine], axis=0)
    bits = n_col.bit_length() - 1
    z_bits = z_len.bit_length() - 1
    n_x = n_col // z_len

    def label(i):
        x = i >> z_bits
        return (x ^ x >> 1) << z_bits | i & (z_len - 1)

    shared = list(range(z_bits - 1, 0, -1))
    orders = ([0] + list(range(bits - 1, z_bits - 1, -1)), list(range(bits - 1, z_bits - 1, -1)) + [0])
    pieces = doubling_gather(packed, "col", label, shared, orders)
    nv, nt = leaf_v.shape[0], leaf_t.shape[0]
    x_order = [x ^ x >> 1 for x in range(n_x)]

    def joined(lo, hi):
        parts = []
        for p in pieces:
            groups = p[:, lo:hi].reshape(n_x, z_len, hi - lo, p.shape[2])
            parts.append(jnp.concatenate([groups[g][None] for g in x_order], axis=0))
        return jnp.concatenate(parts, axis=3).reshape(-1, width)

    v_rows = unit_lower(joined(0, nv))
    t_leaf = joined(nv, nv + nt)
    tree_rows = joined(nv + nt, packed.shape[0])
    refl = [tree_rows[level * width:(level + 1) * width] for level in range(tree_depth)]
    partner_refl = [None] + [swapped(refl[level], "row", level) for level in range(1, tree_depth)]
    coeffs = inner(jnp.triu(t_leaf), inner(v_rows, trailing))
    updated = trailing - matmul(v_rows, coeffs)
    top_rows = updated[:width]
    for level in range(tree_depth):
        top_rows = combine(top_rows, refl[level], partner_refl[level], level)
    return lax.dynamic_update_slice(updated, top_rows, (0, 0))


def solution(mesh):
    in_specs = (
        P("row", "col"),
        P(("row", "col"), None),
        P(("row", "col"), None),
        P(("row", "col"), None),
        P(("row", "col"), None),
    )
    out_specs = P("row", "col")
    z_len = len({d.coords[2] for d in mesh.devices[0].flat})
    return jax.shard_map(functools.partial(local, z_len), mesh=mesh, in_specs=in_specs, out_specs=out_specs, check_vma=False)
```

```python
import functools

import jax
import jax.numpy as jnp
from jax import lax
from jax.sharding import PartitionSpec as P


def swapped(shard, axis, stride):
    return lax.ppermute(shard, axis, [(i, i ^ 1 << stride) for i in range(lax.axis_size(axis))])


def unit_lower(piece):
    rows = lax.broadcasted_iota(jnp.int32, piece.shape, 0)
    cols = lax.broadcasted_iota(jnp.int32, piece.shape, 1)
    return jnp.where(
        rows < cols, jnp.float32(0.0), jnp.where(rows == cols, jnp.float32(1.0), piece)
    )


def inner(left, right):
    return lax.dot_general(
        left,
        right,
        (((0,), (0,)), ((), ())),
        precision=lax.Precision.HIGHEST,
        preferred_element_type=jnp.float32,
    )


def matmul(left, right):
    return jnp.dot(left, right, precision=lax.Precision.HIGHEST, preferred_element_type=jnp.float32)


def doubling_gather(shard, axis, label, shared, orders):
    n = lax.axis_size(axis)
    unlabel = {label(i): i for i in range(n)}
    me = label(lax.axis_index(axis))

    def step(buf, held, bit):
        got = lax.ppermute(buf, axis, [(i, unlabel[label(i) ^ 1 << bit]) for i in range(n)])
        low = (me >> bit) & 1 == 0
        pos = sum(1 for b in held if b > bit)
        return jnp.stack([jnp.where(low, buf, got), jnp.where(low, got, buf)], axis=pos), held[:pos] + [bit] + held[pos:]

    buf, held = shard, []
    for bit in shared:
        buf, held = step(buf, held, bit)
    width = shard.shape[1] // len(orders)
    bufs = [buf[..., j * width:(j + 1) * width] for j in range(len(orders))]
    helds = [held] * len(orders)
    for k in range(len(orders[0]) - 1):
        for j, order in enumerate(orders):
            bufs[j], helds[j] = step(bufs[j], helds[j], order[k])
    pieces = []
    for buf, held, order in zip(bufs, helds, orders):
        bit = order[-1]
        got = lax.ppermute(buf, axis, [(i, unlabel[label(i) ^ 1 << bit]) for i in range(n)])
        low = (me >> bit) & 1 == 0
        pos = sum(1 for b in held if b > bit)
        pieces.append((jnp.where(low, buf, got), jnp.where(low, got, buf), pos))
    return pieces


def combine(top_rows, refl_mine, partner_refl, level):
    lower_side = lax.axis_index("row") // 2**level % 2 == 0
    width = top_rows.shape[0]
    if partner_refl is None:
        incoming = swapped(jnp.concatenate([top_rows, refl_mine], axis=0), "row", level)
        partner_top, partner_refl = incoming[:width], incoming[width:]
    else:
        partner_top = swapped(top_rows, "row", level)
    refl_y = jnp.where(lower_side, refl_mine, partner_refl)
    refl_t = jnp.triu(jnp.where(lower_side, partner_refl, refl_mine))
    lower_top = jnp.where(lower_side, top_rows, partner_top)
    upper_top = jnp.where(lower_side, partner_top, top_rows)
    coeffs = inner(refl_t, lower_top + inner(refl_y, upper_top))
    return jnp.where(lower_side, lower_top - coeffs, upper_top - matmul(refl_y, coeffs))


def local(z_len, trailing, leaf_v, leaf_t, tree_y, tree_t):
    width = leaf_v.shape[1]
    n_col = lax.axis_size("col")
    col = lax.axis_index("col")
    row = lax.axis_index("row")
    tree_depth = tree_y.shape[0] * n_col // width
    shard_level = col * tree_y.shape[0] // width
    tree_mine = jnp.where((row >> shard_level) & 1 == 0, tree_y, tree_t)
    packed = jnp.concatenate([leaf_v, leaf_t, tree_mine], axis=0)
    bits = n_col.bit_length() - 1
    z_bits = z_len.bit_length() - 1
    n_x = n_col // z_len

    def label(i):
        x = i >> z_bits
        return (x ^ x >> 1) << z_bits | i & (z_len - 1)

    shared = list(range(z_bits - 1, 0, -1))
    orders = ([0] + list(range(bits - 1, z_bits - 1, -1)), list(range(bits - 1, z_bits - 1, -1)) + [0])
    pieces = doubling_gather(packed, "col", label, shared, orders)
    nv, nt = leaf_v.shape[0], leaf_t.shape[0]
    x_order = [x ^ x >> 1 for x in range(n_x)]

    def joined(lo, hi):
        parts = []
        for low_half, high_half, pos in pieces:
            p = jnp.stack([low_half[..., lo:hi, :], high_half[..., lo:hi, :]], axis=pos)
            groups = p.reshape(n_x, z_len, hi - lo, p.shape[-1])
            parts.append(jnp.concatenate([groups[g][None] for g in x_order], axis=0))
        return jnp.concatenate(parts, axis=3).reshape(-1, width)

    v_rows = unit_lower(joined(0, nv))
    t_leaf = joined(nv, nv + nt)
    tree_rows = joined(nv + nt, packed.shape[0])
    refl = [tree_rows[level * width:(level + 1) * width] for level in range(tree_depth)]
    partner_refl = [None] + [swapped(refl[level], "row", level) for level in range(1, tree_depth)]
    coeffs = inner(jnp.triu(t_leaf), inner(v_rows, trailing))
    updated = trailing - matmul(v_rows, coeffs)
    top_rows = updated[:width]
    for level in range(tree_depth):
        top_rows = combine(top_rows, refl[level], partner_refl[level], level)
    return lax.dynamic_update_slice(updated, top_rows, (0, 0))


def solution(mesh):
    in_specs = (
        P("row", "col"),
        P(("row", "col"), None),
        P(("row", "col"), None),
        P(("row", "col"), None),
        P(("row", "col"), None),
    )
    out_specs = P("row", "col")
    z_len = len({d.coords[2] for d in mesh.devices[0].flat})
    return jax.shard_map(functools.partial(local, z_len), mesh=mesh, in_specs=in_specs, out_specs=out_specs, check_vma=False)
```

```python
import functools

import jax
import jax.numpy as jnp
from jax import lax
from jax.sharding import PartitionSpec as P


def swapped(shard, axis, stride):
    return lax.ppermute(shard, axis, [(i, i ^ 1 << stride) for i in range(lax.axis_size(axis))])


def unit_lower(piece):
    rows = lax.broadcasted_iota(jnp.int32, piece.shape, 0)
    cols = lax.broadcasted_iota(jnp.int32, piece.shape, 1)
    return jnp.where(
        rows < cols, jnp.float32(0.0), jnp.where(rows == cols, jnp.float32(1.0), piece)
    )


def inner(left, right):
    return lax.dot_general(
        left,
        right,
        (((0,), (0,)), ((), ())),
        precision=lax.Precision.HIGHEST,
        preferred_element_type=jnp.float32,
    )


def matmul(left, right):
    return jnp.dot(left, right, precision=lax.Precision.HIGHEST, preferred_element_type=jnp.float32)


def doubling_gather(shard, axis, label, shared, orders):
    n = lax.axis_size(axis)
    unlabel = {label(i): i for i in range(n)}
    me = label(lax.axis_index(axis))

    def step(buf, held, bit):
        got = lax.ppermute(buf, axis, [(i, unlabel[label(i) ^ 1 << bit]) for i in range(n)])
        low = (me >> bit) & 1 == 0
        pos = sum(1 for b in held if b > bit)
        return jnp.stack([jnp.where(low, buf, got), jnp.where(low, got, buf)], axis=pos), held[:pos] + [bit] + held[pos:]

    buf, held = shard, []
    for bit in shared:
        buf, held = step(buf, held, bit)
    width = shard.shape[1] // len(orders)
    bufs = [buf[..., j * width:(j + 1) * width] for j in range(len(orders))]
    helds = [held] * len(orders)
    for k in range(len(orders[0])):
        for j, order in enumerate(orders):
            bufs[j], helds[j] = step(bufs[j], helds[j], order[k])
    return [b.reshape((n,) + shard.shape[:1] + (width,)) for b in bufs]


def combine(top_rows, refl_mine, partner_refl, level):
    lower_side = lax.axis_index("row") // 2**level % 2 == 0
    width = top_rows.shape[0]
    if partner_refl is None:
        incoming = swapped(jnp.concatenate([top_rows, refl_mine], axis=0), "row", level)
        partner_top, partner_refl = incoming[:width], incoming[width:]
    else:
        partner_top = swapped(top_rows, "row", level)
    refl_y = jnp.where(lower_side, refl_mine, partner_refl)
    refl_t = jnp.triu(jnp.where(lower_side, partner_refl, refl_mine))
    lower_top = jnp.where(lower_side, top_rows, partner_top)
    upper_top = jnp.where(lower_side, partner_top, top_rows)
    coeffs = inner(refl_t, lower_top + inner(refl_y, upper_top))
    return jnp.where(lower_side, lower_top - coeffs, upper_top - matmul(refl_y, coeffs))


def local(z_len, trailing, leaf_v, leaf_t, tree_y, tree_t):
    width = leaf_v.shape[1]
    n_col = lax.axis_size("col")
    col = lax.axis_index("col")
    row = lax.axis_index("row")
    tree_depth = tree_y.shape[0] * n_col // width
    shard_level = col * tree_y.shape[0] // width
    tree_mine = jnp.where((row >> shard_level) & 1 == 0, tree_y, tree_t)
    packed = jnp.concatenate([leaf_v, leaf_t, tree_mine], axis=0)
    bits = n_col.bit_length() - 1
    z_bits = z_len.bit_length() - 1
    n_x = n_col // z_len

    def label(i):
        x = i >> z_bits
        return (x ^ x >> 1) << z_bits | i & (z_len - 1)

    shared = list(range(z_bits - 1, 0, -1))
    orders = ([0] + list(range(bits - 1, z_bits - 1, -1)), list(range(bits - 1, z_bits - 1, -1)) + [0])
    pieces = doubling_gather(packed, "col", label, shared, orders)
    nv, nt = leaf_v.shape[0], leaf_t.shape[0]
    x_order = [x ^ x >> 1 for x in range(n_x)]

    def joined(lo, hi):
        parts = []
        for p in pieces:
            groups = p[:, lo:hi].reshape(n_x, z_len, hi - lo, p.shape[2])
            parts.append(jnp.concatenate([groups[g][None] for g in x_order], axis=0))
        return jnp.concatenate(parts, axis=3).reshape(-1, width)

    v_rows = unit_lower(joined(0, nv))
    t_leaf = joined(nv, nv + nt)
    tree_rows = joined(nv + nt, packed.shape[0])
    refl = [tree_rows[level * width:(level + 1) * width] for level in range(tree_depth)]
    partner_refl = [None] + [swapped(refl[level], "row", level) for level in range(1, tree_depth)]
    coeffs = inner(jnp.triu(t_leaf), inner(v_rows, trailing))
    top_rows = trailing[:width] - matmul(v_rows[:width], coeffs)
    updated = trailing - matmul(v_rows, coeffs)
    for level in range(tree_depth):
        top_rows = combine(top_rows, refl[level], partner_refl[level], level)
    return lax.dynamic_update_slice(updated, top_rows, (0, 0))


def solution(mesh):
    in_specs = (
        P("row", "col"),
        P(("row", "col"), None),
        P(("row", "col"), None),
        P(("row", "col"), None),
        P(("row", "col"), None),
    )
    out_specs = P("row", "col")
    z_len = len({d.coords[2] for d in mesh.devices[0].flat})
    return jax.shard_map(functools.partial(local, z_len), mesh=mesh, in_specs=in_specs, out_specs=out_specs, check_vma=False)
```
